256 devices in a mesh: grp: 8 (over x_hi, y), dev: 32 (over z, x_lo, core).
Axes of the slice: x: 4 (x_hi: 2, x_lo: 2; x = x_hi * 2 + x_lo), y: 4, z: 8, core: 2. Of those that a mesh axis runs over, the one named last changes fastest.
Arguments:
- slab: bfloat16 [16, 8000, 8000], P('grp', 'dev'), may hold values from -2.5 to 2.5
- orbitals: bfloat16 [8000, 640], P('dev'), may hold values from -0.0625 to 0.0625
- hcore: float32 [8000, 8000], P('dev', 'grp'), may hold values from -6 to 6
- metric_inv: float32 [16, 16], replicated, may hold values from -1 to 2, as said below
Outputs:
- fock: float32 [8000, 8000], P('dev', 'grp')
The draws below stay inside these ranges and needn't reach their ends.
Inputs may be any that keep to these rules, and one draw needn't show every extreme that they name: `metric_inv`: symmetric.
All inputs are finite; a program needn't handle non-finite values.
Results may differ from the reference program's by a relative error of at most 0.0065.
Values may be sent and summed in bfloat16 or wider, within the bound.
No kernel may reach another device: no remote copies, remote signals or barrier semaphores. Data moves between devices by JAX's collectives and lax.ppermute only.
A program may use at most 192 MiB of HBM per device.

```python
import math
import jax
import jax.numpy as jnp
from jax import lax

N = 8000
NOCC = 640
NAUX = 16


def draw_metric_inv(key, part):
    key_off, key_diag = jax.random.split(key)
    normal_draw = jnp.clip(jax.random.normal(key_off, (NAUX, NAUX), jnp.float32), -3.0, 3.0)
    symmetric = (normal_draw + normal_draw.T) * (0.3 / math.sqrt(NAUX))
    diag_values = jax.random.uniform(key_diag, (NAUX,), jnp.float32, 1.0, 1.5)
    identity = jnp.eye(NAUX, dtype=jnp.float32)
    return symmetric * (1.0 - identity) + identity * diag_values[None, :]


def spiked(drawn, own_key, source, target, shards_of, factor):
    def block_of(dim):
        return (jnp.arange(drawn.shape[dim]) // (drawn.shape[dim] // shards_of)).reshape((-1,) + (1,) * (drawn.ndim - 1 - dim))

    first = jax.random.permutation(own_key, shards_of)[block_of(target)]
    other_side = (block_of(target) + shards_of // 2) % shards_of
    return jnp.where((block_of(source) == first) | (block_of(source) == other_side), factor * drawn, drawn)


def level_of(own_key, shape, pieces, low, top_value):
    def one(dim, blocks):
        heights = jax.random.uniform(jax.random.fold_in(jax.random.fold_in(own_key, 6), dim), (blocks,), jnp.float32, low / len(pieces), top_value / len(pieces))
        return jnp.repeat(jnp.exp(heights), shape[dim] // blocks).reshape((-1,) + (1,) * (len(shape) - dim - 1))

    level = one(*pieces[0])
    for cut in pieces[1:]:
        level = level * one(*cut)
    return level


def bell_draw(rng, shape, width, bound, cuts=(), kind=jnp.bfloat16):
    gain = level_of(rng, shape, cuts, -0.22, 0.18) if cuts else 1.0
    values = jax.random.normal(rng, shape, jnp.float32) * width * gain
    return jnp.minimum(jnp.maximum(values, -bound), bound).astype(kind)


def noise_with(key, shape, width, limit, shards, heavy, held_as=jnp.bfloat16):
    entries = width * jax.random.normal(key, shape, jnp.float32)
    if shards:
        entries = entries * level_of(key, shape, shards, -0.22, 0.18)
    return jnp.clip(spiked(entries, jax.random.fold_in(key, 3), *heavy), -limit, limit).astype(held_as)


def setup_inputs(seed: int = 0) -> dict:
    streams_of = jax.random.split(jax.random.key(seed), 5)
    slab = noise_with(streams_of[0], (NAUX, N, N), 0.12, 2.5, ((0, 8), (1, 32)), (0, 2, 8, 2.0))
    orbitals = bell_draw(streams_of[1], (N, NOCC), N ** -0.5, 0.0625, ((0, 32),))
    hcore = bell_draw(streams_of[2], (N, N), 1.0, 6.0, ((0, 32), (1, 8)), jnp.float32)
    metric_inv = draw_metric_inv(jax.random.fold_in(streams_of[4], 71), 0)
    return dict(slab=slab, orbitals=orbitals, hcore=hcore, metric_inv=metric_inv)


def reference(slab, orbitals, hcore, metric_inv):
    half_done = jnp.stack([jnp.dot(slab[aux_index], orbitals, preferred_element_type=jnp.float32).astype(jnp.bfloat16) for aux_index in range(NAUX)])
    aux_density = jnp.sum(half_done.astype(jnp.float32) * orbitals.astype(jnp.float32)[None], axis=(1, 2))
    fit_coef = jnp.dot(metric_inv, aux_density, precision=lax.Precision.HIGHEST)
    coulomb = jnp.zeros((N, N), jnp.float32)
    for aux_index in range(NAUX):
        coulomb = coulomb + fit_coef[aux_index] * slab[aux_index].astype(jnp.float32)
    half_flat = jnp.transpose(half_done, (1, 0, 2)).reshape(N, NAUX * NOCC)
    exchange_mat = lax.dot_general(half_flat, half_flat, (((1,), (1,)), ((), ())), preferred_element_type=jnp.float32)
    return hcore + 2.0 * coulomb - exchange_mat
```

```python
import jax
import jax.numpy as jnp
from jax import lax
from jax.sharding import PartitionSpec as P


def shards(slab, orbitals, hcore, metric_inv):
    aux_count = slab.shape[0]
    row_count = slab.shape[1]
    full_width = slab.shape[2]
    occ_count = orbitals.shape[1]
    slab_flat = slab.reshape(aux_count * row_count, full_width)
    half_done = jnp.dot(
        slab_flat,
        lax.all_gather(orbitals, "dev", axis=0, tiled=True),
        preferred_element_type=jnp.float32,
    )
    half_done = half_done.astype(jnp.bfloat16).reshape(aux_count, row_count, occ_count)
    aux_density = jnp.sum(
        half_done.astype(jnp.float32) * orbitals.astype(jnp.float32)[None], axis=(1, 2)
    )
    group_index = lax.axis_index("grp")
    group_density = lax.psum(aux_density, "dev")
    density_all = lax.all_gather(group_density, "grp", axis=0, tiled=True)
    fit_coef = jnp.dot(metric_inv, density_all, precision=lax.Precision.HIGHEST)
    half_flat = jnp.transpose(half_done, (1, 0, 2)).reshape(row_count, aux_count * occ_count)
    exchange_part = lax.dot_general(
        half_flat,
        lax.all_gather(half_flat, "dev", axis=0, tiled=True),
        (((1,), (1,)), ((), ())),
        preferred_element_type=jnp.float32,
    )
    local_coef = lax.dynamic_slice_in_dim(fit_coef, group_index * aux_count, aux_count)
    coulomb_part = jnp.zeros((row_count, full_width), jnp.float32)
    for aux_index in range(aux_count):
        coulomb_part = coulomb_part + local_coef[aux_index] * slab[aux_index].astype(jnp.float32)
    group_count = lax.psum(1, "grp")
    partial = (2.0 * coulomb_part - exchange_part).astype(jnp.bfloat16)
    partial = partial.reshape(row_count, group_count, full_width // group_count)
    pieces = lax.all_to_all(partial, "grp", 1, 1, tiled=True)
    reduced = jnp.sum(pieces.astype(jnp.float32), axis=1)
    fock = hcore + reduced
    return fock


def solution(mesh):
    return jax.shard_map(
        shards,
        mesh=mesh,
        in_specs=(P("grp", "dev", None), P("dev", None), P("dev", "grp"), P()),
        out_specs=P("dev", "grp"),
        check_vma=False,
    )
```

```python
import jax
import jax.numpy as jnp
from jax import lax
from jax.sharding import PartitionSpec as P


def shards(slab, orbitals, hcore, metric_inv):
    aux_count = slab.shape[0]
    row_count = slab.shape[1]
    full_width = slab.shape[2]
    occ_count = orbitals.shape[1]
    slab_flat = slab.reshape(aux_count * row_count, full_width)
    half_done = jnp.dot(
        slab_flat,
        lax.all_gather(orbitals, "dev", axis=0, tiled=True),
        preferred_element_type=jnp.float32,
    )
    half_done = half_done.astype(jnp.bfloat16).reshape(aux_count, row_count, occ_count)
    aux_density = jnp.sum(
        half_done.astype(jnp.float32) * orbitals.astype(jnp.float32)[None], axis=(1, 2)
    )
    group_index = lax.axis_index("grp")
    group_count = lax.psum(1, "grp")
    density_slots = jnp.zeros((group_count, aux_count), jnp.float32)
    density_slots = lax.dynamic_update_index_in_dim(density_slots, aux_density, group_index, 0)
    density_all = lax.psum(density_slots, ("grp", "dev")).reshape(group_count * aux_count)
    fit_coef = jnp.dot(metric_inv, density_all, precision=lax.Precision.HIGHEST)
    half_flat = jnp.transpose(half_done, (1, 0, 2)).reshape(row_count, aux_count * occ_count)
    exchange_part = lax.dot_general(
        half_flat,
        lax.all_gather(half_flat, "dev", axis=0, tiled=True),
        (((1,), (1,)), ((), ())),
        preferred_element_type=jnp.float32,
    )
    local_coef = lax.dynamic_slice_in_dim(fit_coef, group_index * aux_count, aux_count)
    coulomb_part = jnp.zeros((row_count, full_width), jnp.float32)
    for aux_index in range(aux_count):
        coulomb_part = coulomb_part + local_coef[aux_index] * slab[aux_index].astype(jnp.float32)
    partial = (2.0 * coulomb_part - exchange_part).astype(jnp.bfloat16)
    partial = partial.reshape(row_count, group_count, full_width // group_count)
    pieces = lax.all_to_all(partial, "grp", 1, 1, tiled=True)
    reduced = jnp.sum(pieces.astype(jnp.float32), axis=1)
    fock = hcore + reduced
    return fock


def solution(mesh):
    return jax.shard_map(
        shards,
        mesh=mesh,
        in_specs=(P("grp", "dev", None), P("dev", None), P("dev", "grp"), P()),
        out_specs=P("dev", "grp"),
        check_vma=False,
    )
```

```python
import jax
import jax.numpy as jnp
from jax import lax
from jax.sharding import PartitionSpec as P

TILE_ROWS = 256


def shards(slab, orbitals, hcore, metric_inv):
    aux_count = slab.shape[0]
    row_count = slab.shape[1]
    full_width = slab.shape[2]
    occ_count = orbitals.shape[1]
    slab_flat = slab.reshape(aux_count * row_count, full_width)
    half_done = jnp.dot(
        slab_flat,
        lax.all_gather(orbitals, "dev", axis=0, tiled=True),
        preferred_element_type=jnp.float32,
    )
    half_done = half_done.astype(jnp.bfloat16).reshape(aux_count, row_count, occ_count)
    aux_density = jnp.sum(
        half_done.astype(jnp.float32) * orbitals.astype(jnp.float32)[None], axis=(1, 2)
    )
    group_index = lax.axis_index("grp")
    group_count = lax.psum(1, "grp")
    density_slots = jnp.zeros((group_count, aux_count), jnp.float32)
    density_slots = lax.dynamic_update_index_in_dim(density_slots, aux_density, group_index, 0)
    density_all = lax.psum(density_slots, ("grp", "dev")).reshape(group_count * aux_count)
    fit_coef = jnp.dot(metric_inv, density_all, precision=lax.Precision.HIGHEST)
    half_flat = jnp.transpose(half_done, (1, 0, 2)).reshape(row_count, aux_count * occ_count)
    dev_count = full_width // row_count
    tile = -(-row_count // TILE_ROWS) * TILE_ROWS
    half_padded = jnp.pad(half_flat, ((0, tile - row_count), (0, 0)))
    exchange_part = lax.dot_general(
        half_flat,
        lax.all_gather(half_padded, "dev", axis=0, tiled=True),
        (((1,), (1,)), ((), ())),
        preferred_element_type=jnp.float32,
    )
    local_coef = lax.dynamic_slice_in_dim(fit_coef, group_index * aux_count, aux_count)
    coulomb_part = jnp.zeros((row_count, full_width), jnp.float32)
    for aux_index in range(aux_count):
        coulomb_part = coulomb_part + local_coef[aux_index] * slab[aux_index].astype(jnp.float32)
    coulomb_part = jnp.pad(
        coulomb_part.reshape(row_count, dev_count, row_count), ((0, 0), (0, 0), (0, tile - row_count))
    ).reshape(row_count, dev_count * tile)
    partial = (2.0 * coulomb_part - exchange_part).astype(jnp.bfloat16)
    partial = partial.reshape(row_count, group_count, dev_count * tile // group_count)
    pieces = lax.all_to_all(partial, "grp", 1, 1, tiled=True)
    reduced = jnp.sum(pieces.astype(jnp.float32), axis=1)
    reduced = reduced.reshape(row_count, dev_count // group_count, tile)[:, :, :row_count]
    reduced = reduced.reshape(row_count, full_width // group_count)
    fock = hcore + reduced
    return fock


def solution(mesh):
    return jax.shard_map(
        shards,
        mesh=mesh,
        in_specs=(P("grp", "dev", None), P("dev", None), P("dev", "grp"), P()),
        out_specs=P("dev", "grp"),
        check_vma=False,
    )
```

```python
import jax
import jax.numpy as jnp
from jax import lax
from jax.sharding import PartitionSpec as P
from jax.experimental.layout import Layout, with_layout_constraint


def shards(slab, orbitals, hcore, metric_inv):
    aux_count = slab.shape[0]
    row_count = slab.shape[1]
    full_width = slab.shape[2]
    occ_count = orbitals.shape[1]
    slab_flat = slab.reshape(aux_count * row_count, full_width)
    half_done = jnp.dot(
        slab_flat,
        lax.all_gather(orbitals, "dev", axis=0, tiled=True),
        preferred_element_type=jnp.float32,
    )
    half_done = half_done.astype(jnp.bfloat16).reshape(aux_count, row_count, occ_count)
    aux_density = jnp.sum(
        half_done.astype(jnp.float32) * orbitals.astype(jnp.float32)[None], axis=(1, 2)
    )
    group_index = lax.axis_index("grp")
    group_density = lax.psum(aux_density, "dev")
    density_all = lax.all_gather(group_density, "grp", axis=0, tiled=True)
    fit_coef = jnp.dot(metric_inv, density_all, precision=lax.Precision.HIGHEST)
    half_flat = jnp.transpose(half_done, (1, 0, 2)).reshape(row_count, aux_count * occ_count)
    exchange_part = lax.dot_general(
        half_flat,
        lax.all_gather(half_flat, "dev", axis=0, tiled=True),
        (((1,), (1,)), ((), ())),
        preferred_element_type=jnp.float32,
    )
    local_coef = lax.dynamic_slice_in_dim(fit_coef, group_index * aux_count, aux_count)
    coulomb_part = jnp.zeros((row_count, full_width), jnp.float32)
    for aux_index in range(aux_count):
        coulomb_part = coulomb_part + local_coef[aux_index] * slab[aux_index].astype(jnp.float32)
    group_count = lax.psum(1, "grp")
    partial = (2.0 * coulomb_part - exchange_part).astype(jnp.bfloat16)
    partial = with_layout_constraint(partial, Layout((0, 1)))
    partial = partial.reshape(row_count, group_count, full_width // group_count)
    pieces = lax.all_to_all(partial, "grp", 1, 1, tiled=True)
    reduced = jnp.sum(pieces.astype(jnp.float32), axis=1)
    fock = hcore + reduced
    return fock


def solution(mesh):
    return jax.shard_map(
        shards,
        mesh=mesh,
        in_specs=(P("grp", "dev", None), P("dev", None), P("dev", "grp"), P()),
        out_specs=P("dev", "grp"),
        check_vma=False,
    )
```

```python
import jax
import jax.numpy as jnp
from jax import lax
from jax.sharding import PartitionSpec as P

TILE_ROWS = 256


def shards(slab, orbitals, hcore, metric_inv):
    aux_count = slab.shape[0]
    row_count = slab.shape[1]
    full_width = slab.shape[2]
    occ_count = orbitals.shape[1]
    slab_flat = slab.reshape(aux_count * row_count, full_width)
    half_done = jnp.dot(
        slab_flat,
        lax.all_gather(orbitals, "dev", axis=0, tiled=True),
        preferred_element_type=jnp.float32,
    )
    half_done = half_done.astype(jnp.bfloat16).reshape(aux_count, row_count, occ_count)
    aux_density = jnp.sum(
        half_done.astype(jnp.float32) * orbitals.astype(jnp.float32)[None], axis=(1, 2)
    )
    group_index = lax.axis_index("grp")
    group_density = lax.psum(aux_density, "dev")
    density_all = lax.all_gather(group_density, "grp", axis=0, tiled=True)
    fit_coef = jnp.dot(metric_inv, density_all, precision=lax.Precision.HIGHEST)
    half_flat = jnp.transpose(half_done, (1, 0, 2)).reshape(row_count, aux_count * occ_count)
    dev_count = full_width // row_count
    group_count = lax.psum(1, "grp")
    tile = -(-row_count // TILE_ROWS) * TILE_ROWS
    local_coef = lax.dynamic_slice_in_dim(fit_coef, group_index * aux_count, aux_count)
    coulomb_part = jnp.zeros((row_count, full_width), jnp.float32)
    for aux_index in range(aux_count):
        coulomb_part = coulomb_part + local_coef[aux_index] * slab[aux_index].astype(jnp.float32)
    coulomb_pieces = lax.all_to_all(
        (2.0 * coulomb_part).astype(jnp.bfloat16).reshape(row_count, group_count, full_width // group_count),
        "grp", 1, 1, tiled=True,
    )
    half_padded = jnp.pad(half_flat, ((0, tile - row_count), (0, 0)))
    exchange_part = lax.dot_general(
        half_flat,
        lax.all_gather(half_padded, "dev", axis=0, tiled=True),
        (((1,), (1,)), ((), ())),
        preferred_element_type=jnp.float32,
    )
    exchange_pieces = lax.all_to_all(
        exchange_part.astype(jnp.bfloat16).reshape(row_count, group_count, dev_count * tile // group_count),
        "grp", 1, 1, tiled=True,
    )
    exchange_sum = jnp.sum(exchange_pieces.astype(jnp.float32), axis=1)
    exchange_sum = exchange_sum.reshape(row_count, dev_count // group_count, tile)[:, :, :row_count]
    reduced = jnp.sum(coulomb_pieces.astype(jnp.float32), axis=1) - exchange_sum.reshape(
        row_count, full_width // group_count
    )
    fock = hcore + reduced
    return fock


def solution(mesh):
    return jax.shard_map(
        shards,
        mesh=mesh,
        in_specs=(P("grp", "dev", None), P("dev", None), P("dev", "grp"), P()),
        out_specs=P("dev", "grp"),
        check_vma=False,
    )
```

```python
import jax
import jax.numpy as jnp
from jax import lax
from jax.sharding import PartitionSpec as P
from jax.experimental.layout import Layout, with_layout_constraint

TILE_ROWS = 256


def shards(slab, orbitals, hcore, metric_inv):
    aux_count = slab.shape[0]
    row_count = slab.shape[1]
    full_width = slab.shape[2]
    occ_count = orbitals.shape[1]
    slab_flat = slab.reshape(aux_count * row_count, full_width)
    half_done = jnp.dot(
        slab_flat,
        lax.all_gather(orbitals, "dev", axis=0, tiled=True),
        preferred_element_type=jnp.float32,
    )
    half_done = half_done.astype(jnp.bfloat16).reshape(aux_count, row_count, occ_count)
    aux_density = jnp.sum(
        half_done.astype(jnp.float32) * orbitals.astype(jnp.float32)[None], axis=(1, 2)
    )
    group_index = lax.axis_index("grp")
    group_density = lax.psum(aux_density, "dev")
    density_all = lax.all_gather(group_density, "grp", axis=0, tiled=True)
    fit_coef = jnp.dot(metric_inv, density_all, precision=lax.Precision.HIGHEST)
    half_flat = jnp.transpose(half_done, (1, 0, 2)).reshape(row_count, aux_count * occ_count)
    dev_count = full_width // row_count
    group_count = lax.psum(1, "grp")
    tile = -(-row_count // TILE_ROWS) * TILE_ROWS
    local_coef = lax.dynamic_slice_in_dim(fit_coef, group_index * aux_count, aux_count)
    coulomb_part = jnp.zeros((row_count, full_width), jnp.float32)
    for aux_index in range(aux_count):
        coulomb_part = coulomb_part + local_coef[aux_index] * slab[aux_index].astype(jnp.float32)
    coulomb_sent = with_layout_constraint((2.0 * coulomb_part).astype(jnp.bfloat16), Layout((0, 1)))
    coulomb_pieces = lax.all_to_all(
        coulomb_sent.reshape(row_count, group_count, full_width // group_count),
        "grp", 1, 1, tiled=True,
    )
    half_padded = jnp.pad(half_flat, ((0, tile - row_count), (0, 0)))
    exchange_part = lax.dot_general(
        half_flat,
        lax.all_gather(half_padded, "dev", axis=0, tiled=True),
        (((1,), (1,)), ((), ())),
        preferred_element_type=jnp.float32,
    )
    exchange_pieces = lax.all_to_all(
        exchange_part.astype(jnp.bfloat16).reshape(row_count, group_count, dev_count * tile // group_count),
        "grp", 1, 1, tiled=True,
    )
    exchange_sum = jnp.sum(exchange_pieces.astype(jnp.float32), axis=1)
    exchange_sum = exchange_sum.reshape(row_count, dev_count // group_count, tile)[:, :, :row_count]
    reduced = jnp.sum(coulomb_pieces.astype(jnp.float32), axis=1) - exchange_sum.reshape(
        row_count, full_width // group_count
    )
    fock = hcore + reduced
    return fock


def solution(mesh):
    return jax.shard_map(
        shards,
        mesh=mesh,
        in_specs=(P("grp", "dev", None), P("dev", None), P("dev", "grp"), P()),
        out_specs=P("dev", "grp"),
        check_vma=False,
    )
```
